256 devices in a mesh: dp: 8 (over z_hi, x), seq: 32 (over y, z_lo, core).
Axes of the slice: x: 4, y: 4, z: 8 (z_hi: 2, z_lo: 4; z = z_hi * 4 + z_lo), core: 2. Of those that a mesh axis runs over, the one named last changes fastest.
Arguments:
- inputs: bfloat16 [8, 32768, 1024], P('dp', 'seq'), may hold values from -6 to 6
- cotangent: bfloat16 [8, 32768, 1024], P('dp', 'seq'), may hold values from -4 to 4
- factor_one: bfloat16 [32, 1024, 1024], P('seq'), may hold values from -0.1875 to 0.1875
- factor_two: bfloat16 [32, 1024, 1024], P('seq'), may hold values from -0.1875 to 0.1875
Outputs:
- mixed: bfloat16 [8, 32768, 1024], P('dp', 'seq')
- grad_input: bfloat16 [8, 32768, 1024], P('dp', 'seq')
- grad_one: float32 [32, 1024, 1024], P('seq', 'dp')
- grad_two: float32 [32, 1024, 1024], P('seq', 'dp')
The draws below stay inside these ranges and needn't reach their ends.
All inputs are finite; a program needn't handle non-finite values.
Results may differ from the reference program's by a relative error of at most 0.014.
Values may be sent and summed in bfloat16 or wider, within the bound.
No kernel may reach another device: no remote copies, remote signals or barrier semaphores. Data moves between devices by JAX's collectives and lax.ppermute only.
A program may use at most 128 MiB of HBM per device.

```python
import jax
import jax.numpy as jnp
from jax import lax

D = 1024
BLK = 1024
SEQS_DEV = 1
BATCH = 8
NBLK = 32
L = 32768
N_DP = 8


def levels(stream_key, dims, split, smallest, high):
    def one(position, blocks):
        draws = jax.random.uniform(jax.random.fold_in(jax.random.fold_in(stream_key, 6), position), (blocks,), jnp.float32, smallest / len(split), high / len(split))
        return jnp.repeat(jnp.exp(draws), dims[position] // blocks).reshape((-1,) + (1,) * (len(dims) - position - 1))

    level = one(*split[0])
    for cut in split[1:]:
        level = level * one(*cut)
    return level


def noise(key, dims, deviation, limit, shards=(), dtype=jnp.bfloat16):
    result = deviation * jax.random.normal(key, dims, jnp.float32)
    if shards:
        result = result * levels(key, dims, shards, -0.22, 0.18)
    return jnp.clip(result, -limit, limit).astype(dtype)


def setup_inputs(seed: int = 0) -> dict:
    key_of = jax.random.split(jax.random.key(seed), 5)
    inputs = noise(key_of[0], (BATCH, L, D), 1.0, 6.0, ((0, 8), (1, 32)))
    cotangent = noise(key_of[1], (BATCH, L, D), 0.5, 4.0, ((0, 8), (1, 32)))
    factor_one = noise(key_of[2], (NBLK, BLK, BLK), BLK ** -0.5, 0.1875, ((0, 32),))
    factor_two = noise(key_of[3], (NBLK, BLK, BLK), BLK ** -0.5, 0.1875, ((0, 32),))
    return {"inputs": inputs, "cotangent": cotangent, "factor_one": factor_one, "factor_two": factor_two}


def to_moved(data):
    seqs = data.shape[0]
    parts = data.reshape(seqs, NBLK, NBLK, BLK // NBLK, D)
    return jnp.transpose(parts, (0, 2, 3, 1, 4)).reshape(seqs, NBLK, BLK, D)


def from_moved(data):
    seqs = data.shape[0]
    parts = data.reshape(seqs, NBLK, BLK // NBLK, NBLK, D)
    return jnp.transpose(parts, (0, 3, 1, 2, 4)).reshape(seqs, NBLK, BLK, D)


def one_group(inputs, cotangent, factor_one, factor_two):
    seqs = inputs.shape[0]
    xb = inputs.reshape(seqs, NBLK, BLK, D)
    dyb = cotangent.reshape(seqs, NBLK, BLK, D)
    fone = factor_one.astype(jnp.float32)
    ftwo = factor_two.astype(jnp.float32)
    first = jnp.einsum("mkj,smjc->smkc", fone, xb.astype(jnp.float32)).astype(jnp.bfloat16)
    moved = to_moved(first)
    second = jnp.einsum("jpq,sjqc->sjpc", ftwo, moved.astype(jnp.float32)).astype(jnp.bfloat16)
    monarch = from_moved(second)
    mixed = (xb.astype(jnp.float32) * monarch.astype(jnp.float32)).astype(jnp.bfloat16)
    gated = (dyb.astype(jnp.float32) * xb.astype(jnp.float32)).astype(jnp.bfloat16)
    gated_moved = to_moved(gated)
    part_two = jnp.einsum("sjpc,sjqc->jpq", gated_moved.astype(jnp.float32), moved.astype(jnp.float32))
    back_two = jnp.einsum("jpq,sjpc->sjqc", ftwo, gated_moved.astype(jnp.float32)).astype(jnp.bfloat16)
    back_moved = from_moved(back_two)
    part_one = jnp.einsum("smkc,smjc->mkj", back_moved.astype(jnp.float32), xb.astype(jnp.float32))
    grad_input = dyb.astype(jnp.float32) * monarch.astype(jnp.float32)
    grad_input = grad_input + jnp.einsum("mkj,smkc->smjc", fone, back_moved.astype(jnp.float32))
    return (mixed.reshape(seqs, L, D), grad_input.astype(jnp.bfloat16).reshape(seqs, L, D),
            part_one.astype(jnp.bfloat16), part_two.astype(jnp.bfloat16))


def reference(inputs, cotangent, factor_one, factor_two):
    xs = inputs.reshape(N_DP, SEQS_DEV, L, D)
    dys = cotangent.reshape(N_DP, SEQS_DEV, L, D)

    def step(carry, pair):
        mixed, grad_input, part_one, part_two = one_group(pair[0], pair[1], factor_one, factor_two)
        total_one = carry[0] + part_one.astype(jnp.float32)
        total_two = carry[1] + part_two.astype(jnp.float32)
        return (total_one, total_two), (mixed, grad_input)

    start = (jnp.zeros((NBLK, BLK, BLK), jnp.float32), jnp.zeros((NBLK, BLK, BLK), jnp.float32))
    totals, outs = lax.scan(step, start, (xs, dys))
    mixed = outs[0].reshape(BATCH, L, D)
    grad_input = outs[1].reshape(BATCH, L, D)
    return (mixed, grad_input, totals[0], totals[1])
```

```python
import numpy as np
import jax
import jax.numpy as jnp
from jax import lax
from jax.sharding import PartitionSpec as P


def _dp_rings(mesh):
    devs = np.asarray(mesh.devices)
    names = list(mesh.axis_names)
    col = devs.reshape(devs.shape[names.index("dp")], -1) if names.index("dp") == 0 else devs.T
    ndp = col.shape[0]
    try:
        zs = [tuple(col[d, 0].coords)[2] for d in range(ndp)]
        ring = sum(1 for z in zs if z == zs[0])
        if ndp % ring or any(zs[d] != zs[(d // ring) * ring] for d in range(ndp)):
            ring = ndp
    except Exception:
        ring = ndp
    return ring


def _dp_reduce(part, ring):
    ndp = lax.axis_size("dp")
    groups = ndp // ring
    rows = part.shape[0] // ndp
    width = part.shape[1]
    d = lax.axis_index("dp")
    hi = d // ring
    lo = d % ring
    chunks = part.reshape(groups, ring, rows, width)
    acc = lax.dynamic_index_in_dim(chunks, lo, axis=1, keepdims=False).astype(jnp.float32)
    for s in range(1, ring):
        piece = lax.dynamic_index_in_dim(chunks, (lo + s) % ring, axis=1, keepdims=False)
        perm = [(g * ring + t, g * ring + (t + s) % ring) for g in range(groups) for t in range(ring)]
        acc = acc + lax.ppermute(piece, "dp", perm).astype(jnp.float32)
    own = lax.dynamic_index_in_dim(acc, hi, axis=0, keepdims=False)
    for s in range(1, groups):
        piece = lax.dynamic_index_in_dim(acc, (hi + s) % groups, axis=0, keepdims=False)
        perm = [(g * ring + t, ((g + s) % groups) * ring + t) for g in range(groups) for t in range(ring)]
        own = own + lax.ppermute(piece, "dp", perm)
    return own


def local(inputs, cotangent, factor_one, factor_two, ring):
    seqs, block, width = inputs.shape
    count = lax.axis_size("seq")
    rows = block // count
    fone = factor_one[0]
    ftwo = factor_two[0]
    xfull = inputs.astype(jnp.float32)
    dyfull = cotangent.astype(jnp.float32)
    first = jnp.einsum("kj,sjc->skc", fone, inputs, preferred_element_type=jnp.float32).astype(
        jnp.bfloat16
    )
    gated = (dyfull * xfull).astype(jnp.bfloat16)
    out1 = jnp.stack([first, gated]).reshape(2 * seqs, count, rows, 1, width)
    in1 = lax.all_to_all(out1, "seq", split_axis=1, concat_axis=3, tiled=True)
    in1 = in1.reshape(2, seqs, block, width)
    moved = in1[0]
    gated_moved = in1[1]
    second = jnp.einsum("pq,sqc->spc", ftwo, moved, preferred_element_type=jnp.float32).astype(
        jnp.bfloat16
    )
    back_two = jnp.einsum(
        "pq,spc->sqc", ftwo, gated_moved, preferred_element_type=jnp.float32
    ).astype(jnp.bfloat16)
    part_two = jnp.einsum("spc,sqc->pq", gated_moved, moved, preferred_element_type=jnp.float32)
    grad_two = _dp_reduce(part_two.astype(jnp.bfloat16), ring)
    out2 = jnp.stack([second, back_two]).reshape(2 * seqs, 1, rows, count, width)
    in2 = lax.all_to_all(out2, "seq", split_axis=3, concat_axis=1, tiled=True)
    in2 = in2.reshape(2, seqs, block, width)
    monarch = in2[0]
    back_moved = in2[1]
    mfull = monarch.astype(jnp.float32)
    mixed = (xfull * mfull).astype(jnp.bfloat16)
    part_one = jnp.einsum("skc,sjc->kj", back_moved, inputs, preferred_element_type=jnp.float32)
    grad_one = _dp_reduce(part_one.astype(jnp.bfloat16), ring)
    spread = jnp.einsum("kj,skc->sjc", fone, back_moved, preferred_element_type=jnp.float32)
    grad_input = (dyfull * mfull + spread).astype(jnp.bfloat16)
    return (mixed, grad_input, grad_one[None], grad_two[None])


def solution(mesh):
    ring = _dp_rings(mesh)
    in_specs = (
        P("dp", "seq", None),
        P("dp", "seq", None),
        P("seq", None, None),
        P("seq", None, None),
    )
    out_specs = (
        P("dp", "seq", None),
        P("dp", "seq", None),
        P("seq", "dp", None),
        P("seq", "dp", None),
    )
    body = lambda a, b, c, d: local(a, b, c, d, ring)
    return jax.shard_map(body, mesh=mesh, in_specs=in_specs, out_specs=out_specs, check_vma=False)
```

```python
import numpy as np
import jax
import jax.numpy as jnp
from jax import lax
from jax.sharding import PartitionSpec as P


def _dp_rings(mesh):
    devs = np.asarray(mesh.devices)
    names = list(mesh.axis_names)
    col = devs.reshape(devs.shape[names.index("dp")], -1) if names.index("dp") == 0 else devs.T
    ndp = col.shape[0]
    try:
        zs = [tuple(col[d, 0].coords)[2] for d in range(ndp)]
        ring = sum(1 for z in zs if z == zs[0])
        if ndp % ring or any(zs[d] != zs[(d // ring) * ring] for d in range(ndp)):
            ring = ndp
    except Exception:
        ring = ndp
    return ring


def _dp_reduce(part, ring):
    ndp = lax.axis_size("dp")
    groups = ndp // ring
    rows = part.shape[0] // ndp
    width = part.shape[1]
    d = lax.axis_index("dp")
    hi = d // ring
    lo = d % ring
    chunks = part.reshape(groups, ring, rows, width)
    acc = lax.dynamic_index_in_dim(chunks, lo, axis=1, keepdims=False).astype(jnp.float32)
    for s in range(1, ring):
        piece = lax.dynamic_index_in_dim(chunks, (lo + s) % ring, axis=1, keepdims=False)
        perm = [(g * ring + t, g * ring + (t + s) % ring) for g in range(groups) for t in range(ring)]
        acc = acc + lax.ppermute(piece, "dp", perm).astype(jnp.float32)
    own = lax.dynamic_index_in_dim(acc, hi, axis=0, keepdims=False)
    for s in range(1, groups):
        piece = lax.dynamic_index_in_dim(acc, (hi + s) % groups, axis=0, keepdims=False)
        perm = [(g * ring + t, ((g + s) % groups) * ring + t) for g in range(groups) for t in range(ring)]
        own = own + lax.ppermute(piece.astype(jnp.bfloat16), "dp", perm).astype(jnp.float32)
    return own


def _to_moved(data, count, rows):
    seqs, block, width = data.shape
    out = lax.all_to_all(
        data.reshape(seqs, count, rows, 1, width), "seq", split_axis=1, concat_axis=3, tiled=True
    )
    return out.reshape(seqs, block, width)


def _from_moved(data, count, rows):
    seqs, block, width = data.shape
    out = lax.all_to_all(
        data.reshape(seqs, 1, rows, count, width), "seq", split_axis=3, concat_axis=1, tiled=True
    )
    return out.reshape(seqs, block, width)


def local(inputs, cotangent, factor_one, factor_two, ring):
    seqs, block, width = inputs.shape
    count = lax.axis_size("seq")
    rows = block // count
    fone = factor_one[0]
    ftwo = factor_two[0]
    xfull = inputs.astype(jnp.float32)
    dyfull = cotangent.astype(jnp.float32)
    gated = (dyfull * xfull).astype(jnp.bfloat16)
    first = jnp.einsum("kj,sjc->skc", fone, inputs, preferred_element_type=jnp.float32).astype(
        jnp.bfloat16
    )
    out1 = jnp.stack([first, gated]).reshape(2 * seqs, count, rows, 1, width)
    in1 = lax.all_to_all(out1, "seq", split_axis=1, concat_axis=3, tiled=True)
    in1 = in1.reshape(2, seqs, block, width)
    moved = in1[0]
    gated_moved = in1[1]
    back_two = jnp.einsum(
        "pq,spc->sqc", ftwo, gated_moved, preferred_element_type=jnp.float32
    ).astype(jnp.bfloat16)
    back_moved = _from_moved(back_two, count, rows)
    second = jnp.einsum("pq,sqc->spc", ftwo, moved, preferred_element_type=jnp.float32).astype(
        jnp.bfloat16
    )
    part_two = jnp.einsum("spc,sqc->pq", gated_moved, moved, preferred_element_type=jnp.float32)
    grad_two = _dp_reduce(part_two.astype(jnp.bfloat16), ring)
    part_one = jnp.einsum("skc,sjc->kj", back_moved, inputs, preferred_element_type=jnp.float32)
    part_one, second = lax.optimization_barrier((part_one.astype(jnp.bfloat16), second))
    grad_one = _dp_reduce(part_one, ring)
    monarch = _from_moved(second, count, rows)
    spread = jnp.einsum("kj,skc->sjc", fone, back_moved, preferred_element_type=jnp.float32)
    mfull = monarch.astype(jnp.float32)
    mixed = (xfull * mfull).astype(jnp.bfloat16)
    grad_input = (dyfull * mfull + spread).astype(jnp.bfloat16)
    return (mixed, grad_input, grad_one[None], grad_two[None])


def solution(mesh):
    ring = _dp_rings(mesh)
    in_specs = (
        P("dp", "seq", None),
        P("dp", "seq", None),
        P("seq", None, None),
        P("seq", None, None),
    )
    out_specs = (
        P("dp", "seq", None),
        P("dp", "seq", None),
        P("seq", "dp", None),
        P("seq", "dp", None),
    )
    body = lambda a, b, c, d: local(a, b, c, d, ring)
    return jax.shard_map(body, mesh=mesh, in_specs=in_specs, out_specs=out_specs, check_vma=False)
```

```python
import numpy as np
import jax
import jax.numpy as jnp
from jax import lax
from jax.sharding import PartitionSpec as P
from jax.experimental.layout import Layout, with_layout_constraint


def _rowmajor(x):
    return with_layout_constraint(x, Layout(tuple(range(x.ndim))))


def _dp_rings(mesh):
    devs = np.asarray(mesh.devices)
    names = list(mesh.axis_names)
    col = devs.reshape(devs.shape[names.index("dp")], -1) if names.index("dp") == 0 else devs.T
    ndp = col.shape[0]
    try:
        zs = [tuple(col[d, 0].coords)[2] for d in range(ndp)]
        ring = sum(1 for z in zs if z == zs[0])
        if ndp % ring or any(zs[d] != zs[(d // ring) * ring] for d in range(ndp)):
            ring = ndp
    except Exception:
        ring = ndp
    return ring


def _dp_reduce(part, ring):
    ndp = lax.axis_size("dp")
    groups = ndp // ring
    rows = part.shape[0] // ndp
    width = part.shape[1]
    d = lax.axis_index("dp")
    hi = d // ring
    lo = d % ring
    chunks = part.reshape(groups, ring, rows, width)
    acc = lax.dynamic_index_in_dim(chunks, lo, axis=1, keepdims=False).astype(jnp.float32)
    for s in range(1, ring):
        piece = lax.dynamic_index_in_dim(chunks, (lo + s) % ring, axis=1, keepdims=False)
        perm = [(g * ring + t, g * ring + (t + s) % ring) for g in range(groups) for t in range(ring)]
        acc = acc + lax.ppermute(piece, "dp", perm).astype(jnp.float32)
    own = lax.dynamic_index_in_dim(acc, hi, axis=0, keepdims=False)
    for s in range(1, groups):
        piece = lax.dynamic_index_in_dim(acc, (hi + s) % groups, axis=0, keepdims=False)
        perm = [(g * ring + t, ((g + s) % groups) * ring + t) for g in range(groups) for t in range(ring)]
        own = own + lax.ppermute(piece.astype(jnp.bfloat16), "dp", perm).astype(jnp.float32)
    return own


def _to_moved(data, count, rows):
    seqs, block, width = data.shape
    out = lax.all_to_all(
        data.reshape(seqs, count, rows, 1, width), "seq", split_axis=1, concat_axis=3, tiled=True
    )
    return out.reshape(seqs, block, width)


def _from_moved(data, count, rows):
    seqs, block, width = data.shape
    out = lax.all_to_all(
        data.reshape(seqs, 1, rows, count, width), "seq", split_axis=3, concat_axis=1, tiled=True
    )
    return out.reshape(seqs, block, width)


def local(inputs, cotangent, factor_one, factor_two, ring):
    seqs, block, width = inputs.shape
    count = lax.axis_size("seq")
    rows = block // count
    fone = factor_one[0]
    ftwo = factor_two[0]
    xfull = inputs.astype(jnp.float32)
    dyfull = cotangent.astype(jnp.float32)
    gated = _rowmajor((dyfull * xfull).astype(jnp.bfloat16))
    first = jnp.einsum("kj,sjc->skc", fone, inputs, preferred_element_type=jnp.float32).astype(
        jnp.bfloat16
    )
    out1 = jnp.stack([first, gated]).reshape(2 * seqs, count, rows, 1, width)
    in1 = lax.all_to_all(out1, "seq", split_axis=1, concat_axis=3, tiled=True)
    in1 = in1.reshape(2, seqs, block, width)
    moved = in1[0]
    gated_moved = in1[1]
    back_two = jnp.einsum(
        "pq,spc->sqc", ftwo, gated_moved, preferred_element_type=jnp.float32
    ).astype(jnp.bfloat16)
    back_moved = _from_moved(back_two, count, rows)
    second = jnp.einsum("pq,sqc->spc", ftwo, moved, preferred_element_type=jnp.float32).astype(
        jnp.bfloat16
    )
    part_two = jnp.einsum("spc,sqc->pq", gated_moved, moved, preferred_element_type=jnp.float32)
    grad_two = _dp_reduce(part_two.astype(jnp.bfloat16), ring)
    part_one = jnp.einsum("skc,sjc->kj", back_moved, inputs, preferred_element_type=jnp.float32)
    part_one, second = lax.optimization_barrier((part_one.astype(jnp.bfloat16), second))
    grad_one = _dp_reduce(part_one, ring)
    monarch = _from_moved(second, count, rows)
    spread = _rowmajor(jnp.einsum("kj,skc->sjc", fone, back_moved, preferred_element_type=jnp.float32))
    spread = lax.optimization_barrier(spread)
    mfull = monarch.astype(jnp.float32)
    mixed = _rowmajor((xfull * mfull).astype(jnp.bfloat16))
    grad_input = _rowmajor((dyfull * mfull + spread).astype(jnp.bfloat16))
    return (mixed, grad_input, grad_one[None], grad_two[None])


def solution(mesh):
    ring = _dp_rings(mesh)
    in_specs = (
        P("dp", "seq", None),
        P("dp", "seq", None),
        P("seq", None, None),
        P("seq", None, None),
    )
    out_specs = (
        P("dp", "seq", None),
        P("dp", "seq", None),
        P("seq", "dp", None),
        P("seq", "dp", None),
    )
    body = lambda a, b, c, d: local(a, b, c, d, ring)
    return jax.shard_map(body, mesh=mesh, in_specs=in_specs, out_specs=out_specs, check_vma=False)
```

```python
import numpy as np
import jax
import jax.numpy as jnp
from jax import lax
from jax.sharding import PartitionSpec as P
from jax.experimental.layout import Layout, with_layout_constraint


def _rowmajor(x):
    return with_layout_constraint(x, Layout(tuple(range(x.ndim))))


def _dp_rings(mesh):
    devs = np.asarray(mesh.devices)
    names = list(mesh.axis_names)
    col = devs.reshape(devs.shape[names.index("dp")], -1) if names.index("dp") == 0 else devs.T
    ndp = col.shape[0]
    try:
        zs = [tuple(col[d, 0].coords)[2] for d in range(ndp)]
        ring = sum(1 for z in zs if z == zs[0])
        if ndp % ring or any(zs[d] != zs[(d // ring) * ring] for d in range(ndp)):
            ring = ndp
    except Exception:
        ring = ndp
    return ring


def _dp_reduce(part, ring):
    ndp = lax.axis_size("dp")
    groups = ndp // ring
    rows = part.shape[0] // ndp
    width = part.shape[1]
    d = lax.axis_index("dp")
    hi = d // ring
    lo = d % ring
    chunks = part.reshape(groups, ring, rows, width)
    acc = lax.dynamic_index_in_dim(chunks, lo, axis=1, keepdims=False).astype(jnp.float32)
    for s in range(1, ring):
        piece = lax.dynamic_index_in_dim(chunks, (lo + s) % ring, axis=1, keepdims=False)
        perm = [(g * ring + t, g * ring + (t + s) % ring) for g in range(groups) for t in range(ring)]
        acc = acc + lax.ppermute(piece, "dp", perm).astype(jnp.float32)
    own = lax.dynamic_index_in_dim(acc, hi, axis=0, keepdims=False)
    for s in range(1, groups):
        piece = lax.dynamic_index_in_dim(acc, (hi + s) % groups, axis=0, keepdims=False)
        perm = [(g * ring + t, ((g + s) % groups) * ring + t) for g in range(groups) for t in range(ring)]
        own = own + lax.ppermute(piece.astype(jnp.bfloat16), "dp", perm).astype(jnp.float32)
    return own


def _to_moved(data, count, rows):
    seqs, block, width = data.shape
    out = lax.all_to_all(
        data.reshape(seqs, count, rows, 1, width), "seq", split_axis=1, concat_axis=3, tiled=True
    )
    return out.reshape(seqs, block, width)


def _from_moved(data, count, rows):
    seqs, block, width = data.shape
    out = lax.all_to_all(
        data.reshape(seqs, 1, rows, count, width), "seq", split_axis=3, concat_axis=1, tiled=True
    )
    return out.reshape(seqs, block, width)


def local(inputs, cotangent, factor_one, factor_two, ring):
    seqs, block, width = inputs.shape
    count = lax.axis_size("seq")
    rows = block // count
    fone = factor_one[0]
    ftwo = factor_two[0]
    xfull = inputs.astype(jnp.float32)
    dyfull = cotangent.astype(jnp.float32)
    gated = _rowmajor((dyfull * xfull).astype(jnp.bfloat16))
    first = jnp.einsum("kj,sjc->skc", fone, inputs, preferred_element_type=jnp.float32).astype(
        jnp.bfloat16
    )
    out1 = jnp.stack([first, gated]).reshape(2 * seqs, count, rows, 1, width)
    in1 = lax.all_to_all(out1, "seq", split_axis=1, concat_axis=3, tiled=True)
    in1 = in1.reshape(2, seqs, block, width)
    moved = in1[0]
    gated_moved = in1[1]
    back_two = jnp.einsum(
        "pq,spc->sqc", ftwo, gated_moved, preferred_element_type=jnp.float32
    ).astype(jnp.bfloat16)
    back_moved = _from_moved(back_two, count, rows)
    second = jnp.einsum("pq,sqc->spc", ftwo, moved, preferred_element_type=jnp.float32).astype(
        jnp.bfloat16
    )
    part_two = jnp.einsum("spc,sqc->pq", gated_moved, moved, preferred_element_type=jnp.float32)
    grad_two = _dp_reduce(part_two.astype(jnp.bfloat16), ring)
    part_one = jnp.einsum("skc,sjc->kj", back_moved, inputs, preferred_element_type=jnp.float32)
    part_one, second, grad_two = lax.optimization_barrier(
        (part_one.astype(jnp.bfloat16), second, grad_two)
    )
    grad_one = _dp_reduce(part_one, ring)
    monarch = _from_moved(second, count, rows)
    spread = _rowmajor(jnp.einsum("kj,skc->sjc", fone, back_moved, preferred_element_type=jnp.float32))
    spread = lax.optimization_barrier(spread)
    mfull = monarch.astype(jnp.float32)
    mixed = _rowmajor((xfull * mfull).astype(jnp.bfloat16))
    grad_input = _rowmajor((dyfull * mfull + spread).astype(jnp.bfloat16))
    return (mixed, grad_input, grad_one[None], grad_two[None])


def solution(mesh):
    ring = _dp_rings(mesh)
    in_specs = (
        P("dp", "seq", None),
        P("dp", "seq", None),
        P("seq", None, None),
        P("seq", None, None),
    )
    out_specs = (
        P("dp", "seq", None),
        P("dp", "seq", None),
        P("seq", "dp", None),
        P("seq", "dp", None),
    )
    body = lambda a, b, c, d: local(a, b, c, d, ring)
    return jax.shard_map(body, mesh=mesh, in_specs=in_specs, out_specs=out_specs, check_vma=False)
```

```python
import numpy as np
import jax
import jax.numpy as jnp
from jax import lax
from jax.sharding import PartitionSpec as P
from jax.experimental.layout import Layout, with_layout_constraint


def _rowmajor(x):
    return with_layout_constraint(x, Layout(tuple(range(x.ndim))))


def _dp_rings(mesh):
    devs = np.asarray(mesh.devices)
    names = list(mesh.axis_names)
    col = devs.reshape(devs.shape[names.index("dp")], -1) if names.index("dp") == 0 else devs.T
    ndp = col.shape[0]
    try:
        zs = [tuple(col[d, 0].coords)[2] for d in range(ndp)]
        ring = sum(1 for z in zs if z == zs[0])
        if ndp % ring or any(zs[d] != zs[(d // ring) * ring] for d in range(ndp)):
            ring = ndp
    except Exception:
        ring = ndp
    return ring


def _dp_reduce(part, ring):
    ndp = lax.axis_size("dp")
    groups = ndp // ring
    rows = part.shape[0] // ndp
    width = part.shape[1]
    d = lax.axis_index("dp")
    hi = d // ring
    lo = d % ring
    chunks = part.reshape(groups, ring, rows, width)
    acc = lax.dynamic_index_in_dim(chunks, lo, axis=1, keepdims=False).astype(jnp.float32)
    for s in range(1, ring):
        piece = lax.dynamic_index_in_dim(chunks, (lo + s) % ring, axis=1, keepdims=False)
        perm = [(g * ring + t, g * ring + (t + s) % ring) for g in range(groups) for t in range(ring)]
        acc = acc + lax.ppermute(piece, "dp", perm).astype(jnp.float32)
    own = lax.dynamic_index_in_dim(acc, hi, axis=0, keepdims=False)
    for s in range(1, groups):
        piece = lax.dynamic_index_in_dim(acc, (hi + s) % groups, axis=0, keepdims=False)
        perm = [(g * ring + t, ((g + s) % groups) * ring + t) for g in range(groups) for t in range(ring)]
        own = own + lax.ppermute(piece.astype(jnp.bfloat16), "dp", perm).astype(jnp.float32)
    return own


def _to_moved(data, count, rows):
    seqs, block, width = data.shape
    out = lax.all_to_all(
        data.reshape(seqs, count, rows, 1, width), "seq", split_axis=1, concat_axis=3, tiled=True
    )
    return out.reshape(seqs, block, width)


def _from_moved(data, count, rows):
    seqs, block, width = data.shape
    out = lax.all_to_all(
        data.reshape(seqs, 1, rows, count, width), "seq", split_axis=3, concat_axis=1, tiled=True
    )
    return out.reshape(seqs, block, width)


def local(inputs, cotangent, factor_one, factor_two, ring):
    seqs, block, width = inputs.shape
    count = lax.axis_size("seq")
    rows = block // count
    fone = factor_one[0]
    ftwo = factor_two[0]
    xfull = inputs.astype(jnp.float32)
    dyfull = cotangent.astype(jnp.float32)
    gated = _rowmajor((dyfull * xfull).astype(jnp.bfloat16))
    first = jnp.einsum("kj,sjc->skc", fone, inputs, preferred_element_type=jnp.float32).astype(
        jnp.bfloat16
    )
    out1 = jnp.stack([first, gated]).reshape(2 * seqs, count, rows, 1, width)
    in1 = lax.all_to_all(out1, "seq", split_axis=1, concat_axis=3, tiled=True)
    in1 = in1.reshape(2, seqs, block, width)
    moved = in1[0]
    gated_moved = in1[1]
    back_two = jnp.einsum(
        "pq,spc->sqc", ftwo, gated_moved, preferred_element_type=jnp.float32
    ).astype(jnp.bfloat16)
    back_moved = _from_moved(back_two, count, rows)
    second = jnp.einsum("pq,sqc->spc", ftwo, moved, preferred_element_type=jnp.float32).astype(
        jnp.bfloat16
    )
    part_two = jnp.einsum("spc,sqc->pq", gated_moved, moved, preferred_element_type=jnp.float32)
    grad_two = _dp_reduce(part_two.astype(jnp.bfloat16), ring)
    second, grad_two = lax.optimization_barrier((second, grad_two))
    monarch = _from_moved(second, count, rows)
    part_one = jnp.einsum("skc,sjc->kj", back_moved, inputs, preferred_element_type=jnp.float32)
    grad_one = _dp_reduce(part_one.astype(jnp.bfloat16), ring)
    spread = _rowmajor(jnp.einsum("kj,skc->sjc", fone, back_moved, preferred_element_type=jnp.float32))
    spread = lax.optimization_barrier(spread)
    mfull = monarch.astype(jnp.float32)
    mixed = _rowmajor((xfull * mfull).astype(jnp.bfloat16))
    grad_input = _rowmajor((dyfull * mfull + spread).astype(jnp.bfloat16))
    return (mixed, grad_input, grad_one[None], grad_two[None])


def solution(mesh):
    ring = _dp_rings(mesh)
    in_specs = (
        P("dp", "seq", None),
        P("dp", "seq", None),
        P("seq", None, None),
        P("seq", None, None),
    )
    out_specs = (
        P("dp", "seq", None),
        P("dp", "seq", None),
        P("seq", "dp", None),
        P("seq", "dp", None),
    )
    body = lambda a, b, c, d: local(a, b, c, d, ring)
    return jax.shard_map(body, mesh=mesh, in_specs=in_specs, out_specs=out_specs, check_vma=False)
```

```python
import numpy as np
import jax
import jax.numpy as jnp
from jax import lax
from jax.sharding import PartitionSpec as P
from jax.experimental.layout import Layout, with_layout_constraint


def _rowmajor(x):
    return with_layout_constraint(x, Layout(tuple(range(x.ndim))))


def _dp_rings(mesh):
    devs = np.asarray(mesh.devices)
    names = list(mesh.axis_names)
    col = devs.reshape(devs.shape[names.index("dp")], -1) if names.index("dp") == 0 else devs.T
    ndp = col.shape[0]
    try:
        zs = [tuple(col[d, 0].coords)[2] for d in range(ndp)]
        ring = sum(1 for z in zs if z == zs[0])
        if ndp % ring or any(zs[d] != zs[(d // ring) * ring] for d in range(ndp)):
            ring = ndp
    except Exception:
        ring = ndp
    return ring


def _dp_reduce(part, ring):
    ndp = lax.axis_size("dp")
    groups = ndp // ring
    rows = part.shape[0] // ndp
    width = part.shape[1]
    d = lax.axis_index("dp")
    hi = d // ring
    lo = d % ring
    chunks = part.reshape(groups, ring, rows, width)
    acc = lax.dynamic_index_in_dim(chunks, lo, axis=1, keepdims=False).astype(jnp.float32)
    for s in range(1, ring):
        piece = lax.dynamic_index_in_dim(chunks, (lo + s) % ring, axis=1, keepdims=False)
        perm = [(g * ring + t, g * ring + (t + s) % ring) for g in range(groups) for t in range(ring)]
        acc = acc + lax.ppermute(piece, "dp", perm).astype(jnp.float32)
    own = lax.dynamic_index_in_dim(acc, hi, axis=0, keepdims=False)
    for s in range(1, groups):
        piece = lax.dynamic_index_in_dim(acc, (hi + s) % groups, axis=0, keepdims=False)
        perm = [(g * ring + t, ((g + s) % groups) * ring + t) for g in range(groups) for t in range(ring)]
        own = own + lax.ppermute(piece.astype(jnp.bfloat16), "dp", perm).astype(jnp.float32)
    return own


def _exchange(data, count):
    axis = data.ndim - 3
    return lax.all_to_all(data, "seq", split_axis=axis, concat_axis=axis, tiled=True)


def local(inputs, cotangent, factor_one, factor_two, ring):
    seqs, block, width = inputs.shape
    count = lax.axis_size("seq")
    rows = block // count
    fone = factor_one[0]
    ftwo = factor_two[0].reshape(rows, count, rows, count).transpose(1, 0, 3, 2).reshape(block, block)
    xfull = inputs.astype(jnp.float32)
    dyfull = cotangent.astype(jnp.float32)
    gated = _rowmajor((dyfull * xfull).astype(jnp.bfloat16))
    first = jnp.einsum("kj,sjc->skc", fone, inputs, preferred_element_type=jnp.float32).astype(
        jnp.bfloat16
    )
    out1 = jnp.stack([first, gated]).reshape(2 * seqs, count, rows, width)
    in1 = _exchange(out1, count).reshape(2, seqs, block, width)
    moved = in1[0]
    gated_moved = in1[1]
    back_two = jnp.einsum(
        "pq,spc->sqc", ftwo, gated_moved, preferred_element_type=jnp.float32
    ).astype(jnp.bfloat16)
    back_moved = _exchange(back_two.reshape(seqs, count, rows, width), count)
    back_moved = back_moved.reshape(seqs, block, width)
    second = jnp.einsum("pq,sqc->spc", ftwo, moved, preferred_element_type=jnp.float32).astype(
        jnp.bfloat16
    )
    part_two = jnp.einsum(
        "smrc,sntc->rmtn",
        gated_moved.reshape(seqs, count, rows, width),
        moved.reshape(seqs, count, rows, width),
        preferred_element_type=jnp.float32,
    ).reshape(block, block)
    grad_two = _dp_reduce(part_two.astype(jnp.bfloat16), ring)
    second, grad_two = lax.optimization_barrier((second, grad_two))
    monarch = _exchange(second.reshape(seqs, count, rows, width), count)
    monarch = monarch.reshape(seqs, block, width)
    part_one = jnp.einsum("skc,sjc->kj", back_moved, inputs, preferred_element_type=jnp.float32)
    grad_one = _dp_reduce(part_one.astype(jnp.bfloat16), ring)
    spread = _rowmajor(jnp.einsum("kj,skc->sjc", fone, back_moved, preferred_element_type=jnp.float32))
    spread = lax.optimization_barrier(spread)
    mfull = monarch.astype(jnp.float32)
    mixed = _rowmajor((xfull * mfull).astype(jnp.bfloat16))
    grad_input = _rowmajor((dyfull * mfull + spread).astype(jnp.bfloat16))
    return (mixed, grad_input, grad_one[None], grad_two[None])


def solution(mesh):
    ring = _dp_rings(mesh)
    in_specs = (
        P("dp", "seq", None),
        P("dp", "seq", None),
        P("seq", None, None),
        P("seq", None, None),
    )
    out_specs = (
        P("dp", "seq", None),
        P("dp", "seq", None),
        P("seq", "dp", None),
        P("seq", "dp", None),
    )
    body = lambda a, b, c, d: local(a, b, c, d, ring)
    return jax.shard_map(body, mesh=mesh, in_specs=in_specs, out_specs=out_specs, check_vma=False)
```

```python
import numpy as np
import jax
import jax.numpy as jnp
from jax import lax
from jax.sharding import PartitionSpec as P
from jax.experimental.layout import Layout, with_layout_constraint


def _rowmajor(x):
    return with_layout_constraint(x, Layout(tuple(range(x.ndim))))


def _dp_rings(mesh):
    devs = np.asarray(mesh.devices)
    names = list(mesh.axis_names)
    col = devs.reshape(devs.shape[names.index("dp")], -1) if names.index("dp") == 0 else devs.T
    ndp = col.shape[0]
    try:
        zs = [tuple(col[d, 0].coords)[2] for d in range(ndp)]
        ring = sum(1 for z in zs if z == zs[0])
        if ndp % ring or any(zs[d] != zs[(d // ring) * ring] for d in range(ndp)):
            ring = ndp
    except Exception:
        ring = ndp
    return ring


def _z_relays(mesh, ring):
    devs = np.asarray(mesh.devices)
    if tuple(mesh.axis_names) != ("dp", "seq") or devs.shape[0] != 2 * ring:
        return None
    try:
        where = {}
        for d in range(devs.shape[0]):
            for q in range(devs.shape[1]):
                dev = devs[d, q]
                where[tuple(dev.coords) + (dev.core_on_chip,)] = d * devs.shape[1] + q
        nz = 1 + max(k[2] for k in where)
        half = nz // 2
        for d in range(devs.shape[0]):
            for q in range(devs.shape[1]):
                a, b = devs[d, q], devs[(d + ring) % devs.shape[0], q]
                ca, cb = tuple(a.coords), tuple(b.coords)
                if ca[:2] != cb[:2] or a.core_on_chip != b.core_on_chip or (cb[2] - ca[2]) % nz != half:
                    return None

        def shift(step):
            out = []
            for k, i in where.items():
                t = (k[0], k[1], (k[2] + step) % nz, k[3])
                out.append((i, where[t]))
            return out

        return (shift(1), shift(half - 1), shift(-1), shift(1 - half))
    except Exception:
        return None


def _dp_reduce(part, ring, relays=None):
    ndp = lax.axis_size("dp")
    groups = ndp // ring
    rows = part.shape[0] // ndp
    width = part.shape[1]
    d = lax.axis_index("dp")
    hi = d // ring
    lo = d % ring
    chunks = part.reshape(groups, ring, rows, width)
    acc = lax.dynamic_index_in_dim(chunks, lo, axis=1, keepdims=False).astype(jnp.float32)
    for s in range(1, ring):
        piece = lax.dynamic_index_in_dim(chunks, (lo + s) % ring, axis=1, keepdims=False)
        perm = [(g * ring + t, g * ring + (t + s) % ring) for g in range(groups) for t in range(ring)]
        acc = acc + lax.ppermute(piece, "dp", perm).astype(jnp.float32)
    own = lax.dynamic_index_in_dim(acc, hi, axis=0, keepdims=False)
    if relays is not None and groups == 2:
        piece = lax.dynamic_index_in_dim(acc, 1 - hi, axis=0, keepdims=False).astype(jnp.bfloat16)
        cut = rows // 2
        up = lax.ppermute(piece[:cut], ("dp", "seq"), relays[0])
        up = lax.ppermute(up, ("dp", "seq"), relays[1])
        down = lax.ppermute(piece[cut:], ("dp", "seq"), relays[2])
        down = lax.ppermute(down, ("dp", "seq"), relays[3])
        return own + jnp.concatenate([up, down]).astype(jnp.float32)
    for s in range(1, groups):
        piece = lax.dynamic_index_in_dim(acc, (hi + s) % groups, axis=0, keepdims=False)
        perm = [(g * ring + t, ((g + s) % groups) * ring + t) for g in range(groups) for t in range(ring)]
        own = own + lax.ppermute(piece.astype(jnp.bfloat16), "dp", perm).astype(jnp.float32)
    return own


def _to_moved(data, count, rows):
    seqs, block, width = data.shape
    out = lax.all_to_all(
        data.reshape(seqs, count, rows, 1, width), "seq", split_axis=1, concat_axis=3, tiled=True
    )
    return out.reshape(seqs, block, width)


def _from_moved(data, count, rows):
    seqs, block, width = data.shape
    return _from_sendbuf(_sendbuf(data, count, rows), count)


def _sendbuf(data, count, rows):
    seqs, block, width = data.shape
    return jnp.swapaxes(data.reshape(seqs, rows, count, width), 1, 2)


def _from_sendbuf(buf, count):
    seqs, _, rows, width = buf.shape
    out = lax.all_to_all(buf, "seq", split_axis=1, concat_axis=1, tiled=True)
    return out.reshape(seqs, count * rows, width)


def local(inputs, cotangent, factor_one, factor_two, ring, relays):
    seqs, block, width = inputs.shape
    count = lax.axis_size("seq")
    rows = block // count
    fone = factor_one[0]
    ftwo = factor_two[0]
    xfull = inputs.astype(jnp.float32)
    dyfull = cotangent.astype(jnp.float32)
    gated = _rowmajor((dyfull * xfull).astype(jnp.bfloat16))
    first = jnp.einsum("kj,sjc->skc", fone, inputs, preferred_element_type=jnp.float32).astype(
        jnp.bfloat16
    )
    out1 = jnp.stack([first, gated]).reshape(2 * seqs, count, rows, 1, width)
    in1 = lax.all_to_all(out1, "seq", split_axis=1, concat_axis=3, tiled=True)
    in1 = in1.reshape(2, seqs, block, width)
    moved = in1[0]
    gated_moved = in1[1]
    back_two = jnp.einsum(
        "pq,spc->sqc", ftwo, gated_moved, preferred_element_type=jnp.float32
    ).astype(jnp.bfloat16)
    back_moved = _from_moved(back_two, count, rows)
    second = jnp.einsum("pq,sqc->spc", ftwo, moved, preferred_element_type=jnp.float32).astype(
        jnp.bfloat16
    )
    part_two = jnp.einsum("spc,sqc->pq", gated_moved, moved, preferred_element_type=jnp.float32)
    grad_two = _dp_reduce(part_two.astype(jnp.bfloat16), ring, relays)
    second = _sendbuf(second, count, rows)
    second, back_moved, grad_two = lax.optimization_barrier((second, back_moved, grad_two))
    monarch = _from_sendbuf(second, count)
    part_one = jnp.einsum("skc,sjc->kj", back_moved, inputs, preferred_element_type=jnp.float32)
    grad_one = _dp_reduce(part_one.astype(jnp.bfloat16), ring, relays)
    spread = _rowmajor(jnp.einsum("kj,skc->sjc", fone, back_moved, preferred_element_type=jnp.float32))
    spread = lax.optimization_barrier(spread)
    mfull = monarch.astype(jnp.float32)
    mixed = _rowmajor((xfull * mfull).astype(jnp.bfloat16))
    grad_input = _rowmajor((dyfull * mfull + spread).astype(jnp.bfloat16))
    return (mixed, grad_input, grad_one[None], grad_two[None])


def solution(mesh):
    ring = _dp_rings(mesh)
    relays = _z_relays(mesh, ring)
    in_specs = (
        P("dp", "seq", None),
        P("dp", "seq", None),
        P("seq", None, None),
        P("seq", None, None),
    )
    out_specs = (
        P("dp", "seq", None),
        P("dp", "seq", None),
        P("seq", "dp", None),
        P("seq", "dp", None),
    )
    body = lambda a, b, c, d: local(a, b, c, d, ring, relays)
    return jax.shard_map(body, mesh=mesh, in_specs=in_specs, out_specs=out_specs, check_vma=False)
```

```python
import numpy as np
import jax
import jax.numpy as jnp
from jax import lax
from jax.sharding import PartitionSpec as P
from jax.experimental.layout import Layout, with_layout_constraint


def _rowmajor(x):
    return with_layout_constraint(x, Layout(tuple(range(x.ndim))))


def _dp_rings(mesh):
    devs = np.asarray(mesh.devices)
    names = list(mesh.axis_names)
    col = devs.reshape(devs.shape[names.index("dp")], -1) if names.index("dp") == 0 else devs.T
    ndp = col.shape[0]
    try:
        zs = [tuple(col[d, 0].coords)[2] for d in range(ndp)]
        ring = sum(1 for z in zs if z == zs[0])
        if ndp % ring or any(zs[d] != zs[(d // ring) * ring] for d in range(ndp)):
            ring = ndp
    except Exception:
        ring = ndp
    return ring


def _dp_reduce(part, ring):
    ndp = lax.axis_size("dp")
    groups = ndp // ring
    rows = part.shape[0] // ndp
    width = part.shape[1]
    d = lax.axis_index("dp")
    hi = d // ring
    lo = d % ring
    chunks = part.reshape(groups, ring, rows, width)
    acc = lax.dynamic_index_in_dim(chunks, lo, axis=1, keepdims=False).astype(jnp.float32)
    for s in range(1, ring):
        piece = lax.dynamic_index_in_dim(chunks, (lo + s) % ring, axis=1, keepdims=False)
        perm = [(g * ring + t, g * ring + (t + s) % ring) for g in range(groups) for t in range(ring)]
        acc = acc + lax.ppermute(piece, "dp", perm).astype(jnp.float32)
    own = lax.dynamic_index_in_dim(acc, hi, axis=0, keepdims=False)
    for s in range(1, groups):
        piece = lax.dynamic_index_in_dim(acc, (hi + s) % groups, axis=0, keepdims=False)
        perm = [(g * ring + t, ((g + s) % groups) * ring + t) for g in range(groups) for t in range(ring)]
        own = own + lax.ppermute(piece.astype(jnp.bfloat16), "dp", perm).astype(jnp.float32)
    return own


def _exchange(data, count):
    axis = data.ndim - 3
    return lax.all_to_all(data, "seq", split_axis=axis, concat_axis=axis, tiled=True)


def local(inputs, cotangent, factor_one, factor_two, ring):
    seqs, block, width = inputs.shape
    count = lax.axis_size("seq")
    rows = block // count
    fone = factor_one[0]
    pp = jnp.arange(block)
    pick = (pp[None, :] == ((pp % rows) * count + pp // rows)[:, None]).astype(jnp.bfloat16)
    ftwo = jnp.dot(pick, factor_two[0], preferred_element_type=jnp.float32).astype(jnp.bfloat16)
    ftwo = jnp.dot(ftwo, pick.T, preferred_element_type=jnp.float32).astype(jnp.bfloat16)
    xfull = inputs.astype(jnp.float32)
    dyfull = cotangent.astype(jnp.float32)
    gated = _rowmajor((dyfull * xfull).astype(jnp.bfloat16))
    first = jnp.einsum("kj,sjc->skc", fone, inputs, preferred_element_type=jnp.float32).astype(
        jnp.bfloat16
    )
    out1 = jnp.stack([first, gated]).reshape(2 * seqs, count, rows, width)
    in1 = _exchange(out1, count).reshape(2, seqs, block, width)
    moved = in1[0]
    gated_moved = in1[1]
    back_two = jnp.einsum(
        "pq,spc->sqc", ftwo, gated_moved, preferred_element_type=jnp.float32
    ).astype(jnp.bfloat16)
    back_moved = _exchange(back_two.reshape(seqs, count, rows, width), count)
    back_moved = back_moved.reshape(seqs, block, width)
    second = jnp.einsum("pq,sqc->spc", ftwo, moved, preferred_element_type=jnp.float32).astype(
        jnp.bfloat16
    )
    part_two = jnp.einsum("spc,sqc->pq", gated_moved, moved, preferred_element_type=jnp.float32)
    part_two = jnp.dot(pick.T, part_two.astype(jnp.bfloat16), preferred_element_type=jnp.float32)
    part_two = jnp.dot(part_two.astype(jnp.bfloat16), pick, preferred_element_type=jnp.float32)
    grad_two = _dp_reduce(part_two.astype(jnp.bfloat16), ring)
    second, grad_two = lax.optimization_barrier((second, grad_two))
    monarch = _exchange(second.reshape(seqs, count, rows, width), count)
    monarch = monarch.reshape(seqs, block, width)
    part_one = jnp.einsum("skc,sjc->kj", back_moved, inputs, preferred_element_type=jnp.float32)
    grad_one = _dp_reduce(part_one.astype(jnp.bfloat16), ring)
    spread = _rowmajor(jnp.einsum("kj,skc->sjc", fone, back_moved, preferred_element_type=jnp.float32))
    spread = lax.optimization_barrier(spread)
    mfull = monarch.astype(jnp.float32)
    mixed = _rowmajor((xfull * mfull).astype(jnp.bfloat16))
    grad_input = _rowmajor((dyfull * mfull + spread).astype(jnp.bfloat16))
    return (mixed, grad_input, grad_one[None], grad_two[None])


def solution(mesh):
    ring = _dp_rings(mesh)
    in_specs = (
        P("dp", "seq", None),
        P("dp", "seq", None),
        P("seq", None, None),
        P("seq", None, None),
    )
    out_specs = (
        P("dp", "seq", None),
        P("dp", "seq", None),
        P("seq", "dp", None),
        P("seq", "dp", None),
    )
    body = lambda a, b, c, d: local(a, b, c, d, ring)
    return jax.shard_map(body, mesh=mesh, in_specs=in_specs, out_specs=out_specs, check_vma=False)
```

```python
import numpy as np
import jax
import jax.numpy as jnp
from jax import lax
from jax.sharding import PartitionSpec as P
from jax.experimental.layout import Layout, with_layout_constraint


def _rowmajor(x):
    return with_layout_constraint(x, Layout(tuple(range(x.ndim))))


def _dp_rings(mesh):
    devs = np.asarray(mesh.devices)
    names = list(mesh.axis_names)
    col = devs.reshape(devs.shape[names.index("dp")], -1) if names.index("dp") == 0 else devs.T
    ndp = col.shape[0]
    try:
        zs = [tuple(col[d, 0].coords)[2] for d in range(ndp)]
        ring = sum(1 for z in zs if z == zs[0])
        if ndp % ring or any(zs[d] != zs[(d // ring) * ring] for d in range(ndp)):
            ring = ndp
    except Exception:
        ring = ndp
    return ring


def _dp_reduce(part, ring):
    ndp = lax.axis_size("dp")
    groups = ndp // ring
    rows = part.shape[0] // ndp
    width = part.shape[1]
    d = lax.axis_index("dp")
    hi = d // ring
    lo = d % ring
    chunks = part.reshape(groups, ring, rows, width)
    acc = lax.dynamic_index_in_dim(chunks, lo, axis=1, keepdims=False).astype(jnp.float32)
    for s in range(1, ring):
        piece = lax.dynamic_index_in_dim(chunks, (lo + s) % ring, axis=1, keepdims=False)
        perm = [(g * ring + t, g * ring + (t + s) % ring) for g in range(groups) for t in range(ring)]
        acc = acc + lax.ppermute(piece, "dp", perm).astype(jnp.float32)
    return acc


def _dp_finish(acc, ring):
    ndp = lax.axis_size("dp")
    groups = ndp // ring
    hi = lax.axis_index("dp") // ring
    own = lax.dynamic_index_in_dim(acc, hi, axis=0, keepdims=False)
    for s in range(1, groups):
        piece = lax.dynamic_index_in_dim(acc, (hi + s) % groups, axis=0, keepdims=False)
        perm = [(g * ring + t, ((g + s) % groups) * ring + t) for g in range(groups) for t in range(ring)]
        own = own + lax.ppermute(piece.astype(jnp.bfloat16), "dp", perm).astype(jnp.float32)
    return own


def _to_moved(data, count, rows):
    seqs, block, width = data.shape
    out = lax.all_to_all(
        data.reshape(seqs, count, rows, 1, width), "seq", split_axis=1, concat_axis=3, tiled=True
    )
    return out.reshape(seqs, block, width)


def _from_moved(data, count, rows):
    seqs, block, width = data.shape
    out = lax.all_to_all(
        data.reshape(seqs, 1, rows, count, width), "seq", split_axis=3, concat_axis=1, tiled=True
    )
    return out.reshape(seqs, block, width)


def local(inputs, cotangent, factor_one, factor_two, ring):
    seqs, block, width = inputs.shape
    count = lax.axis_size("seq")
    rows = block // count
    fone = factor_one[0]
    ftwo = factor_two[0]
    xfull = inputs.astype(jnp.float32)
    dyfull = cotangent.astype(jnp.float32)
    gated = _rowmajor((dyfull * xfull).astype(jnp.bfloat16))
    first = jnp.einsum("kj,sjc->skc", fone, inputs, preferred_element_type=jnp.float32).astype(
        jnp.bfloat16
    )
    out1 = jnp.stack([first, gated]).reshape(2 * seqs, count, rows, 1, width)
    in1 = lax.all_to_all(out1, "seq", split_axis=1, concat_axis=3, tiled=True)
    in1 = in1.reshape(2, seqs, block, width)
    moved = in1[0]
    gated_moved = in1[1]
    back_two = jnp.einsum(
        "pq,spc->sqc", ftwo, gated_moved, preferred_element_type=jnp.float32
    ).astype(jnp.bfloat16)
    back_moved = _from_moved(back_two, count, rows)
    second = jnp.einsum("pq,sqc->spc", ftwo, moved, preferred_element_type=jnp.float32).astype(
        jnp.bfloat16
    )
    part_two = jnp.einsum("spc,sqc->pq", gated_moved, moved, preferred_element_type=jnp.float32)
    acc_two = _dp_reduce(part_two.astype(jnp.bfloat16), ring)
    second, acc_two = lax.optimization_barrier((second, acc_two))
    monarch = _from_moved(second, count, rows)
    part_one = jnp.einsum("skc,sjc->kj", back_moved, inputs, preferred_element_type=jnp.float32)
    acc_one = _dp_reduce(part_one.astype(jnp.bfloat16), ring)
    monarch, acc_one, acc_two = lax.optimization_barrier((monarch, acc_one, acc_two))
    grad_one = _dp_finish(acc_one, ring)
    grad_two = _dp_finish(acc_two, ring)
    spread = _rowmajor(jnp.einsum("kj,skc->sjc", fone, back_moved, preferred_element_type=jnp.float32))
    spread = lax.optimization_barrier(spread)
    mfull = monarch.astype(jnp.float32)
    mixed = _rowmajor((xfull * mfull).astype(jnp.bfloat16))
    grad_input = _rowmajor((dyfull * mfull + spread).astype(jnp.bfloat16))
    return (mixed, grad_input, grad_one[None], grad_two[None])


def solution(mesh):
    ring = _dp_rings(mesh)
    in_specs = (
        P("dp", "seq", None),
        P("dp", "seq", None),
        P("seq", None, None),
        P("seq", None, None),
    )
    out_specs = (
        P("dp", "seq", None),
        P("dp", "seq", None),
        P("seq", "dp", None),
        P("seq", "dp", None),
    )
    body = lambda a, b, c, d: local(a, b, c, d, ring)
    return jax.shard_map(body, mesh=mesh, in_specs=in_specs, out_specs=out_specs, check_vma=False)
```

```python
import numpy as np
import jax
import jax.numpy as jnp
from jax import lax
from jax.sharding import PartitionSpec as P
from jax.experimental.layout import Layout, with_layout_constraint


def _rowmajor(x):
    return with_layout_constraint(x, Layout(tuple(range(x.ndim))))


def _dp_rings(mesh):
    devs = np.asarray(mesh.devices)
    names = list(mesh.axis_names)
    col = devs.reshape(devs.shape[names.index("dp")], -1) if names.index("dp") == 0 else devs.T
    ndp = col.shape[0]
    try:
        zs = [tuple(col[d, 0].coords)[2] for d in range(ndp)]
        ring = sum(1 for z in zs if z == zs[0])
        if ndp % ring or any(zs[d] != zs[(d // ring) * ring] for d in range(ndp)):
            ring = ndp
    except Exception:
        ring = ndp
    return ring


def _dp_reduce(part, ring):
    ndp = lax.axis_size("dp")
    groups = ndp // ring
    rows = part.shape[0] // ndp
    width = part.shape[1]
    d = lax.axis_index("dp")
    hi = d // ring
    lo = d % ring
    chunks = part.reshape(groups, ring, rows, width)
    acc = lax.dynamic_index_in_dim(chunks, lo, axis=1, keepdims=False).astype(jnp.float32)
    for s in range(1, ring):
        piece = lax.dynamic_index_in_dim(chunks, (lo + s) % ring, axis=1, keepdims=False)
        perm = [(g * ring + t, g * ring + (t + s) % ring) for g in range(groups) for t in range(ring)]
        acc = acc + lax.ppermute(piece, "dp", perm).astype(jnp.float32)
    return acc


def _dp_finish(acc, ring):
    ndp = lax.axis_size("dp")
    groups = ndp // ring
    hi = lax.axis_index("dp") // ring
    own = lax.dynamic_index_in_dim(acc, hi, axis=0, keepdims=False)
    for s in range(1, groups):
        piece = lax.dynamic_index_in_dim(acc, (hi + s) % groups, axis=0, keepdims=False)
        perm = [(g * ring + t, ((g + s) % groups) * ring + t) for g in range(groups) for t in range(ring)]
        own = own + lax.ppermute(piece.astype(jnp.bfloat16), "dp", perm).astype(jnp.float32)
    return own


def _to_moved(data, count, rows):
    seqs, block, width = data.shape
    out = lax.all_to_all(
        data.reshape(seqs, count, rows, 1, width), "seq", split_axis=1, concat_axis=3, tiled=True
    )
    return out.reshape(seqs, block, width)


def _from_moved(data, count, rows):
    seqs, block, width = data.shape
    out = lax.all_to_all(
        data.reshape(seqs, 1, rows, count, width), "seq", split_axis=3, concat_axis=1, tiled=True
    )
    return out.reshape(seqs, block, width)


def local(inputs, cotangent, factor_one, factor_two, ring):
    seqs, block, width = inputs.shape
    count = lax.axis_size("seq")
    rows = block // count
    fone = factor_one[0]
    ftwo = factor_two[0]
    xfull = inputs.astype(jnp.float32)
    dyfull = cotangent.astype(jnp.float32)
    gated = _rowmajor((dyfull * xfull).astype(jnp.bfloat16))
    first = jnp.einsum("kj,sjc->skc", fone, inputs, preferred_element_type=jnp.float32).astype(
        jnp.bfloat16
    )
    out1 = jnp.stack([first, gated]).reshape(2 * seqs, count, rows, 1, width)
    in1 = lax.all_to_all(out1, "seq", split_axis=1, concat_axis=3, tiled=True)
    in1 = in1.reshape(2, seqs, block, width)
    moved = in1[0]
    gated_moved = in1[1]
    back_two = jnp.einsum(
        "pq,spc->sqc", ftwo, gated_moved, preferred_element_type=jnp.float32
    ).astype(jnp.bfloat16)
    back_moved = _from_moved(back_two, count, rows)
    second = jnp.einsum("pq,sqc->spc", ftwo, moved, preferred_element_type=jnp.float32).astype(
        jnp.bfloat16
    )
    part_two = jnp.einsum("spc,sqc->pq", gated_moved, moved, preferred_element_type=jnp.float32)
    acc_two = _dp_reduce(part_two.astype(jnp.bfloat16), ring)
    second, acc_two = lax.optimization_barrier((second, acc_two))
    monarch = _from_moved(second, count, rows)
    part_one = jnp.einsum("skc,sjc->kj", back_moved, inputs, preferred_element_type=jnp.float32)
    acc_one = _dp_reduce(part_one.astype(jnp.bfloat16), ring)
    monarch, acc_one, acc_two = lax.optimization_barrier((monarch, acc_one, acc_two))
    both = _dp_finish(jnp.concatenate([acc_one, acc_two], axis=1), ring)
    grad_one = both[: acc_one.shape[1]]
    grad_two = both[acc_one.shape[1] :]
    spread = _rowmajor(jnp.einsum("kj,skc->sjc", fone, back_moved, preferred_element_type=jnp.float32))
    spread = lax.optimization_barrier(spread)
    mfull = monarch.astype(jnp.float32)
    mixed = _rowmajor((xfull * mfull).astype(jnp.bfloat16))
    grad_input = _rowmajor((dyfull * mfull + spread).astype(jnp.bfloat16))
    return (mixed, grad_input, grad_one[None], grad_two[None])


def solution(mesh):
    ring = _dp_rings(mesh)
    in_specs = (
        P("dp", "seq", None),
        P("dp", "seq", None),
        P("seq", None, None),
        P("seq", None, None),
    )
    out_specs = (
        P("dp", "seq", None),
        P("dp", "seq", None),
        P("seq", "dp", None),
        P("seq", "dp", None),
    )
    body = lambda a, b, c, d: local(a, b, c, d, ring)
    return jax.shard_map(body, mesh=mesh, in_specs=in_specs, out_specs=out_specs, check_vma=False)
```

```python
import numpy as np
import jax
import jax.numpy as jnp
from jax import lax
from jax.sharding import PartitionSpec as P
from jax.experimental.layout import Layout, with_layout_constraint


def _rowmajor(x):
    return with_layout_constraint(x, Layout(tuple(range(x.ndim))))


def _dp_rings(mesh):
    devs = np.asarray(mesh.devices)
    names = list(mesh.axis_names)
    col = devs.reshape(devs.shape[names.index("dp")], -1) if names.index("dp") == 0 else devs.T
    ndp = col.shape[0]
    try:
        zs = [tuple(col[d, 0].coords)[2] for d in range(ndp)]
        ring = sum(1 for z in zs if z == zs[0])
        if ndp % ring or any(zs[d] != zs[(d // ring) * ring] for d in range(ndp)):
            ring = ndp
    except Exception:
        ring = ndp
    return ring


def _z_relays(mesh, ring):
    devs = np.asarray(mesh.devices)
    if tuple(mesh.axis_names) != ("dp", "seq") or devs.shape[0] != 2 * ring:
        return None
    try:
        where = {}
        for d in range(devs.shape[0]):
            for q in range(devs.shape[1]):
                dev = devs[d, q]
                where[tuple(dev.coords) + (dev.core_on_chip,)] = d * devs.shape[1] + q
        nz = 1 + max(k[2] for k in where)
        half = nz // 2
        for d in range(devs.shape[0]):
            for q in range(devs.shape[1]):
                a, b = devs[d, q], devs[(d + ring) % devs.shape[0], q]
                ca, cb = tuple(a.coords), tuple(b.coords)
                if ca[:2] != cb[:2] or a.core_on_chip != b.core_on_chip or (cb[2] - ca[2]) % nz != half:
                    return None

        def shift(step):
            out = []
            for k, i in where.items():
                t = (k[0], k[1], (k[2] + step) % nz, k[3])
                out.append((i, where[t]))
            return out

        return (shift(1), shift(half - 1), shift(-1), shift(1 - half))
    except Exception:
        return None


def _dp_reduce(part, ring):
    ndp = lax.axis_size("dp")
    groups = ndp // ring
    rows = part.shape[0] // ndp
    width = part.shape[1]
    d = lax.axis_index("dp")
    hi = d // ring
    lo = d % ring
    chunks = part.reshape(groups, ring, rows, width)
    acc = lax.dynamic_index_in_dim(chunks, lo, axis=1, keepdims=False).astype(jnp.float32)
    for s in range(1, ring):
        piece = lax.dynamic_index_in_dim(chunks, (lo + s) % ring, axis=1, keepdims=False)
        perm = [(g * ring + t, g * ring + (t + s) % ring) for g in range(groups) for t in range(ring)]
        acc = acc + lax.ppermute(piece, "dp", perm).astype(jnp.float32)
    return acc


def _dp_finish(acc, ring, relays=None):
    ndp = lax.axis_size("dp")
    groups = ndp // ring
    hi = lax.axis_index("dp") // ring
    own = lax.dynamic_index_in_dim(acc, hi, axis=0, keepdims=False)
    if relays is not None and groups == 2:
        piece = lax.dynamic_index_in_dim(acc, 1 - hi, axis=0, keepdims=False).astype(jnp.bfloat16)
        cut = piece.shape[0] // 2
        up = lax.ppermute(piece[:cut], ("dp", "seq"), relays[0])
        down = lax.ppermute(piece[cut:], ("dp", "seq"), relays[2])
        up = lax.ppermute(up, ("dp", "seq"), relays[1])
        down = lax.ppermute(down, ("dp", "seq"), relays[3])
        return own + jnp.concatenate([up, down]).astype(jnp.float32)
    for s in range(1, groups):
        piece = lax.dynamic_index_in_dim(acc, (hi + s) % groups, axis=0, keepdims=False)
        perm = [(g * ring + t, ((g + s) % groups) * ring + t) for g in range(groups) for t in range(ring)]
        own = own + lax.ppermute(piece.astype(jnp.bfloat16), "dp", perm).astype(jnp.float32)
    return own


def _to_moved(data, count, rows):
    seqs, block, width = data.shape
    out = lax.all_to_all(
        data.reshape(seqs, count, rows, 1, width), "seq", split_axis=1, concat_axis=3, tiled=True
    )
    return out.reshape(seqs, block, width)


def _from_moved(data, count, rows):
    seqs, block, width = data.shape
    out = lax.all_to_all(
        data.reshape(seqs, 1, rows, count, width), "seq", split_axis=3, concat_axis=1, tiled=True
    )
    return out.reshape(seqs, block, width)


def local(inputs, cotangent, factor_one, factor_two, ring, relays):
    seqs, block, width = inputs.shape
    count = lax.axis_size("seq")
    rows = block // count
    fone = factor_one[0]
    ftwo = factor_two[0]
    xfull = inputs.astype(jnp.float32)
    dyfull = cotangent.astype(jnp.float32)
    gated = _rowmajor((dyfull * xfull).astype(jnp.bfloat16))
    first = jnp.einsum("kj,sjc->skc", fone, inputs, preferred_element_type=jnp.float32).astype(
        jnp.bfloat16
    )
    out1 = jnp.stack([first, gated]).reshape(2 * seqs, count, rows, 1, width)
    in1 = lax.all_to_all(out1, "seq", split_axis=1, concat_axis=3, tiled=True)
    in1 = in1.reshape(2, seqs, block, width)
    moved = in1[0]
    gated_moved = in1[1]
    back_two = jnp.einsum(
        "pq,spc->sqc", ftwo, gated_moved, preferred_element_type=jnp.float32
    ).astype(jnp.bfloat16)
    back_moved = _from_moved(back_two, count, rows)
    second = jnp.einsum("pq,sqc->spc", ftwo, moved, preferred_element_type=jnp.float32).astype(
        jnp.bfloat16
    )
    part_two = jnp.einsum("spc,sqc->pq", gated_moved, moved, preferred_element_type=jnp.float32)
    acc_two = _dp_reduce(part_two.astype(jnp.bfloat16), ring)
    second, acc_two = lax.optimization_barrier((second, acc_two))
    monarch = _from_moved(second, count, rows)
    part_one = jnp.einsum("skc,sjc->kj", back_moved, inputs, preferred_element_type=jnp.float32)
    acc_one = _dp_reduce(part_one.astype(jnp.bfloat16), ring)
    monarch, acc_one, acc_two = lax.optimization_barrier((monarch, acc_one, acc_two))
    both = _dp_finish(jnp.concatenate([acc_one, acc_two], axis=1), ring, relays)
    grad_one = both[: acc_one.shape[1]]
    grad_two = both[acc_one.shape[1] :]
    spread = _rowmajor(jnp.einsum("kj,skc->sjc", fone, back_moved, preferred_element_type=jnp.float32))
    spread = lax.optimization_barrier(spread)
    mfull = monarch.astype(jnp.float32)
    mixed = _rowmajor((xfull * mfull).astype(jnp.bfloat16))
    grad_input = _rowmajor((dyfull * mfull + spread).astype(jnp.bfloat16))
    return (mixed, grad_input, grad_one[None], grad_two[None])


def solution(mesh):
    ring = _dp_rings(mesh)
    relays = _z_relays(mesh, ring)
    in_specs = (
        P("dp", "seq", None),
        P("dp", "seq", None),
        P("seq", None, None),
        P("seq", None, None),
    )
    out_specs = (
        P("dp", "seq", None),
        P("dp", "seq", None),
        P("seq", "dp", None),
        P("seq", "dp", None),
    )
    body = lambda a, b, c, d: local(a, b, c, d, ring, relays)
    return jax.shard_map(body, mesh=mesh, in_specs=in_specs, out_specs=out_specs, check_vma=False)
```

```python
import numpy as np
import jax
import jax.numpy as jnp
from jax import lax
from jax.sharding import PartitionSpec as P
from jax.experimental.layout import Layout, with_layout_constraint


def _rowmajor(x):
    return with_layout_constraint(x, Layout(tuple(range(x.ndim))))


def _dp_rings(mesh):
    devs = np.asarray(mesh.devices)
    names = list(mesh.axis_names)
    col = devs.reshape(devs.shape[names.index("dp")], -1) if names.index("dp") == 0 else devs.T
    ndp = col.shape[0]
    try:
        zs = [tuple(col[d, 0].coords)[2] for d in range(ndp)]
        ring = sum(1 for z in zs if z == zs[0])
        if ndp % ring or any(zs[d] != zs[(d // ring) * ring] for d in range(ndp)):
            ring = ndp
    except Exception:
        ring = ndp
    return ring


def _dp_reduce(part, ring):
    ndp = lax.axis_size("dp")
    groups = ndp // ring
    rows = part.shape[0] // ndp
    width = part.shape[1]
    d = lax.axis_index("dp")
    hi = d // ring
    lo = d % ring
    chunks = part.reshape(groups, ring, rows, width)
    acc = lax.dynamic_index_in_dim(chunks, lo, axis=1, keepdims=False).astype(jnp.float32)
    for s in range(1, ring):
        piece = lax.dynamic_index_in_dim(chunks, (lo + s) % ring, axis=1, keepdims=False)
        perm = [(g * ring + t, g * ring + (t + s) % ring) for g in range(groups) for t in range(ring)]
        acc = acc + lax.ppermute(piece, "dp", perm).astype(jnp.float32)
    return acc


def _dp_finish(acc, ring):
    ndp = lax.axis_size("dp")
    groups = ndp // ring
    hi = lax.axis_index("dp") // ring
    own = lax.dynamic_index_in_dim(acc, hi, axis=0, keepdims=False)
    for s in range(1, groups):
        piece = lax.dynamic_index_in_dim(acc, (hi + s) % groups, axis=0, keepdims=False)
        perm = [(g * ring + t, ((g + s) % groups) * ring + t) for g in range(groups) for t in range(ring)]
        own = own + lax.ppermute(piece.astype(jnp.bfloat16), "dp", perm).astype(jnp.float32)
    return own


def _to_moved(data, count, rows):
    seqs, block, width = data.shape
    out = lax.all_to_all(
        data.reshape(seqs, count, rows, 1, width), "seq", split_axis=1, concat_axis=3, tiled=True
    )
    return out.reshape(seqs, block, width)


def _from_moved(data, count, rows):
    seqs, block, width = data.shape
    out = lax.all_to_all(
        data.reshape(seqs, 1, rows, count, width), "seq", split_axis=3, concat_axis=1, tiled=True
    )
    return out.reshape(seqs, block, width)


def local(inputs, cotangent, factor_one, factor_two, ring):
    seqs, block, width = inputs.shape
    count = lax.axis_size("seq")
    rows = block // count
    fone = factor_one[0]
    ftwo = factor_two[0]
    xfull = inputs.astype(jnp.float32)
    dyfull = cotangent.astype(jnp.float32)
    gated = _rowmajor((dyfull * xfull).astype(jnp.bfloat16))
    first = jnp.einsum("kj,sjc->skc", fone, inputs, preferred_element_type=jnp.float32).astype(
        jnp.bfloat16
    )
    out1 = jnp.stack([first, gated]).reshape(2 * seqs, count, rows, 1, width)
    in1 = lax.all_to_all(out1, "seq", split_axis=1, concat_axis=3, tiled=True)
    in1 = in1.reshape(2, seqs, block, width)
    moved = in1[0]
    gated_moved = in1[1]
    back_two = jnp.einsum(
        "pq,spc->sqc", ftwo, gated_moved, preferred_element_type=jnp.float32
    ).astype(jnp.bfloat16)
    back_moved = _from_moved(back_two, count, rows)
    second = jnp.einsum("pq,sqc->spc", ftwo, moved, preferred_element_type=jnp.float32).astype(
        jnp.bfloat16
    )
    part_two = jnp.einsum("spc,sqc->pq", gated_moved, moved, preferred_element_type=jnp.float32)
    grad_two = _dp_finish(_dp_reduce(part_two.astype(jnp.bfloat16), ring), ring)
    second, grad_two = lax.optimization_barrier((second, grad_two))
    monarch = _from_moved(second, count, rows)
    part_one = jnp.einsum("skc,sjc->kj", back_moved, inputs, preferred_element_type=jnp.float32)
    acc_one = _dp_reduce(part_one.astype(jnp.bfloat16), ring)
    monarch, acc_one = lax.optimization_barrier((monarch, acc_one))
    grad_one = _dp_finish(acc_one, ring)
    spread = _rowmajor(jnp.einsum("kj,skc->sjc", fone, back_moved, preferred_element_type=jnp.float32))
    spread = lax.optimization_barrier(spread)
    mfull = monarch.astype(jnp.float32)
    mixed = _rowmajor((xfull * mfull).astype(jnp.bfloat16))
    grad_input = _rowmajor((dyfull * mfull + spread).astype(jnp.bfloat16))
    return (mixed, grad_input, grad_one[None], grad_two[None])


def solution(mesh):
    ring = _dp_rings(mesh)
    in_specs = (
        P("dp", "seq", None),
        P("dp", "seq", None),
        P("seq", None, None),
        P("seq", None, None),
    )
    out_specs = (
        P("dp", "seq", None),
        P("dp", "seq", None),
        P("seq", "dp", None),
        P("seq", "dp", None),
    )
    body = lambda a, b, c, d: local(a, b, c, d, ring)
    return jax.shard_map(body, mesh=mesh, in_specs=in_specs, out_specs=out_specs, check_vma=False)
```
